256 devices in a mesh: row: 32 (over y_hi, z, core), col: 8 (over y_lo, x).
Axes of the slice: x: 4, y: 4 (y_hi: 2, y_lo: 2; y = y_hi * 2 + y_lo), z: 8, core: 2. Of those that a mesh axis runs over, the one named last changes fastest.
Arguments:
- colloc: bfloat16 [2, 2048, 9216], P(None, 'row'), may hold values from -6 to 6
- coefficients: bfloat16 [2, 9216, 512], P(None, 'row'), may hold values from -0.0625 to 0.0625
- occupied: int32 [2], replicated, may hold values from 256 to 512
- offsets: int32 [2, 2], replicated, may hold values from 0 to 2048
Outputs:
- exchange_matrix: bfloat16 [9216, 2, 9216], P('col', None, 'row')
The draws below stay inside these ranges and needn't reach their ends.
Inputs may be any that keep to these rules, and one draw needn't show every extreme that they name: occupied[s] is the number of occupied orbitals of spin s. offsets[s, k] is the first point of panel k of spin s on the line of 73728 points; both panels lie within the first 3072 points and may intersect.
All inputs are finite; a program needn't handle non-finite values.
Results may differ from the reference program's by a relative error of at most 0.019.
Values may be sent and summed in bfloat16 or wider, within the bound.
No kernel may reach another device: no remote copies, remote signals or barrier semaphores. Data moves between devices by JAX's collectives and lax.ppermute only.
A program may use at most 128 MiB of HBM per device.

```python
import math
import jax
import jax.numpy as jnp
from jax import lax

NB = 9216
OCC = 512
SPINS = 2
PR = 64
PTS = 2048
PANEL = 1024
SCREEN = 128
N_ROW = 32
N_COL = 8


def place_ends(entries, own_key, low, largest):
    index_at = [jax.random.randint(jax.random.fold_in(own_key, axis), (), 0, length) for axis, length in enumerate(entries.shape)]
    main_axis = entries.shape.index(max(entries.shape))
    neighbour = index_at[:main_axis] + [(index_at[main_axis] + 1) % entries.shape[main_axis]] + index_at[main_axis + 1:]
    return entries.at[tuple(index_at)].set(low).at[tuple(neighbour)].set(largest)


def level_of(key, extent, cuts, least, top_value):
    def one(axis_at, blocks):
        heights = jax.random.uniform(jax.random.fold_in(jax.random.fold_in(key, 6), axis_at), (blocks,), jnp.float32, least / len(cuts), top_value / len(cuts))
        return jnp.repeat(jnp.exp(heights), extent[axis_at] // blocks).reshape((-1,) + (1,) * (len(extent) - axis_at - 1))

    gain = one(*cuts[0])
    for cut in cuts[1:]:
        gain = gain * one(*cut)
    return gain


def gaussian(stream_key, dims, scale, reach, pieces=(), held_as=jnp.bfloat16):
    values = scale * jax.random.normal(stream_key, dims, jnp.float32)
    if pieces:
        values = values * level_of(stream_key, dims, pieces, -0.22, 0.18)
    return jnp.clip(values, -reach, reach).astype(held_as)


def setup_inputs(seed: int = 0) -> dict:
    splits = jax.random.split(jax.random.key(seed), 5)
    return {
        "colloc": gaussian(splits[0], (SPINS, PTS, NB), 1.0, 6.0, ((1, 32),)),
        "coefficients": gaussian(splits[1], (SPINS, NB, OCC), NB ** -0.5, 0.0625, ((1, 32),)),
        "occupied": jax.random.randint(splits[2], (SPINS,), OCC // 2, OCC + 1).astype(jnp.int32),
        "offsets": place_ends(jax.random.randint(splits[3], (SPINS, 2), 0, 2 * PANEL + 1), jax.random.fold_in(splits[3], 1), 0, 2 * PANEL).astype(jnp.int32),
    }


def point_positions(point_ids, offsets, panel_len):
    first = jnp.where(point_ids[None, :] // panel_len == 0, offsets[:, 0:1], offsets[:, 1:2])
    return (first + point_ids[None, :] % panel_len).astype(jnp.float32)

def reference(colloc, coefficients, occupied, offsets):
    orbitals = jnp.einsum('spm,smi->spi', colloc.astype(jnp.float32), coefficients.astype(jnp.float32))
    occupied_mask = jnp.arange(OCC, dtype=jnp.int32)[None, :] < occupied[:, None]
    orbitals = jnp.where(occupied_mask[:, None, :], orbitals, 0.0).astype(jnp.bfloat16)
    point_ids = jnp.arange(PTS, dtype=jnp.int32)
    positions = point_positions(point_ids, offsets, PANEL)
    kernel = 1.0 / (1.0 + jnp.abs(positions[:, :, None] - positions[:, None, :]) / SCREEN)
    density = jnp.einsum('spi,sqi->spq', orbitals.astype(jnp.float32), orbitals.astype(jnp.float32))
    mixed_kernel = (kernel * density / OCC).astype(jnp.bfloat16)
    weighted = jnp.einsum('spq,sqn->spn', mixed_kernel.astype(jnp.float32), colloc.astype(jnp.float32)).astype(jnp.bfloat16)
    norm_factor = 1.0 / math.sqrt(PTS)
    sub_rows = PR // N_COL
    left_split = colloc.reshape(SPINS, N_ROW, N_COL, sub_rows, NB)
    right_split = weighted.reshape(SPINS, N_ROW, N_COL, sub_rows, NB)
    result = jnp.zeros((NB, SPINS, NB), jnp.float32)
    for group in range(N_COL):
        left_rows = left_split[:, :, group].astype(jnp.float32)
        right_rows = right_split[:, :, group].astype(jnp.float32)
        group_term = jnp.einsum('sxkm,sxkn->msn', left_rows, right_rows) * norm_factor
        rounded = lax.optimization_barrier(group_term.astype(jnp.bfloat16))
        result = result + rounded.astype(jnp.float32)
    return result.astype(jnp.bfloat16)
```

```python
import math

import jax
import jax.numpy as jnp
from jax import lax
from jax.sharding import PartitionSpec as P


def point_positions(point_ids, offsets, panel_len):
    first = jnp.where(point_ids[None, :] // panel_len == 0, offsets[:, 0:1], offsets[:, 1:2])
    return (first + point_ids[None, :] % panel_len).astype(jnp.float32)


def local(colloc, coefficients, occupied, offsets):
    row_count = lax.axis_size("row")
    col_count = lax.axis_size("col")
    col_index = lax.axis_index("col")
    spin_count, own_points, basis = colloc.shape
    slots = coefficients.shape[2]
    sub_rows = own_points // col_count
    points = own_points * row_count
    panel_len = points // 2
    screen_len = panel_len // 8
    col_width = basis // col_count
    norm_factor = 1.0 / math.sqrt(points)

    own_cols = lax.dynamic_slice_in_dim(colloc, col_index * col_width, col_width, 2)
    basis_cols = lax.all_gather(own_cols, "row", axis=1, tiled=True)

    own_rows = lax.dynamic_slice_in_dim(colloc, col_index * sub_rows, sub_rows, 1)
    regrouped = lax.all_to_all(own_rows, "row", split_axis=2, concat_axis=1, tiled=True)
    partial_value = jnp.einsum(
        "spm,smi->spi", regrouped, coefficients, preferred_element_type=jnp.float32
    )
    summed = lax.psum_scatter(partial_value, "row", scatter_dimension=1, tiled=True)
    occupied_mask = jnp.arange(slots, dtype=jnp.int32)[None, :] < occupied[:, None]
    orbitals_own = jnp.where(occupied_mask[:, None, :], summed, 0.0).astype(jnp.bfloat16)
    orbitals_all = lax.all_gather(orbitals_own, ("row", "col"), axis=1, tiled=True)

    basis_group = lax.all_gather(regrouped, "col", axis=1, tiled=True)
    basis_rows = (
        basis_group.reshape(spin_count, col_count, row_count, sub_rows, -1)
        .transpose(0, 2, 1, 3, 4)
        .reshape(spin_count, points, -1)
    )

    positions = point_positions(jnp.arange(points, dtype=jnp.int32), offsets, panel_len)
    kernel = 1.0 / (1.0 + jnp.abs(positions[:, :, None] - positions[:, None, :]) / screen_len)
    density = jnp.einsum(
        "spi,sqi->spq", orbitals_all, orbitals_all, preferred_element_type=jnp.float32
    )
    mixed_kernel = (kernel * density / slots).astype(jnp.bfloat16)
    weighted = jnp.einsum(
        "spq,sqn->spn", mixed_kernel, basis_rows, preferred_element_type=jnp.float32
    ).astype(jnp.bfloat16)
    return (
        jnp.einsum("spm,spn->msn", basis_cols, weighted, preferred_element_type=jnp.float32)
        * norm_factor
    ).astype(jnp.bfloat16)


def solution(mesh):
    placed = (P(None, "row", None), P(None, "row", None), P(), P())
    return jax.shard_map(
        local, mesh=mesh, in_specs=placed, out_specs=P("col", None, "row"), check_vma=False
    )
```

```python
import math

import jax
import jax.numpy as jnp
from jax import lax
from jax.sharding import PartitionSpec as P


def point_positions(point_ids, offsets, panel_len):
    first = jnp.where(point_ids[None, :] // panel_len == 0, offsets[:, 0:1], offsets[:, 1:2])
    return (first + point_ids[None, :] % panel_len).astype(jnp.float32)


def local(colloc, coefficients, occupied, offsets):
    row_count = lax.axis_size("row")
    col_count = lax.axis_size("col")
    col_index = lax.axis_index("col")
    spin_count, own_points, basis = colloc.shape
    slots = coefficients.shape[2]
    sub_rows = own_points // col_count
    points = own_points * row_count
    panel_len = points // 2
    screen_len = panel_len // 8
    col_width = basis // col_count
    row_width = basis // row_count
    norm_factor = 1.0 / math.sqrt(points)

    own_cols = lax.dynamic_slice_in_dim(colloc, col_index * col_width, col_width, 2)
    basis_cols = lax.all_gather(own_cols, "row", axis=1, tiled=True)

    own_rows = lax.dynamic_slice_in_dim(colloc, col_index * sub_rows, sub_rows, 1)
    send = own_rows.reshape(spin_count, sub_rows, row_count, row_width).transpose(2, 0, 1, 3)
    regrouped = lax.all_to_all(send, "row", split_axis=0, concat_axis=0, tiled=True)
    basis_all = lax.all_gather(regrouped, "col", axis=0)

    partial_value = jnp.einsum(
        "xspm,smi->xspi", regrouped, coefficients, preferred_element_type=jnp.float32
    )
    received = lax.all_to_all(partial_value, "row", split_axis=0, concat_axis=0, tiled=True)
    summed = jnp.sum(received, axis=0)
    occupied_mask = jnp.arange(slots, dtype=jnp.int32)[None, :] < occupied[:, None]
    orbitals_own = jnp.where(occupied_mask[:, None, :], summed, 0.0).astype(jnp.bfloat16)
    spread = jnp.broadcast_to(orbitals_own[None], (row_count,) + orbitals_own.shape)
    orbitals_group = lax.all_to_all(spread, "row", split_axis=0, concat_axis=0, tiled=True)
    orbitals_all = lax.all_gather(orbitals_group, "col", axis=0)

    def flat(x):
        return jnp.moveaxis(x, 2, 0).reshape(spin_count, points, x.shape[-1])

    orbitals_perm = flat(orbitals_all)
    basis_perm = flat(basis_all)
    ids = jnp.arange(points, dtype=jnp.int32)
    group_of, rest = ids // (row_count * sub_rows), ids % (row_count * sub_rows)
    perm_ids = rest // sub_rows * own_points + group_of * sub_rows + rest % sub_rows
    positions = point_positions(perm_ids, offsets, panel_len)
    kernel = 1.0 / (1.0 + jnp.abs(positions[:, :, None] - positions[:, None, :]) / screen_len)
    density = jnp.einsum(
        "spi,sqi->spq", orbitals_perm, orbitals_perm, preferred_element_type=jnp.float32
    )
    mixed_kernel = (kernel * density / slots).astype(jnp.bfloat16)
    weighted = jnp.einsum(
        "spq,sqn->spn", mixed_kernel, basis_perm, preferred_element_type=jnp.float32
    ).astype(jnp.bfloat16)
    weighted = (
        weighted.reshape(spin_count, col_count, row_count, sub_rows, -1)
        .transpose(0, 2, 1, 3, 4)
        .reshape(spin_count, points, -1)
    )
    return (
        jnp.einsum("spm,spn->msn", basis_cols, weighted, preferred_element_type=jnp.float32)
        * norm_factor
    ).astype(jnp.bfloat16)


def solution(mesh):
    placed = (P(None, "row", None), P(None, "row", None), P(), P())
    return jax.shard_map(
        local, mesh=mesh, in_specs=placed, out_specs=P("col", None, "row"), check_vma=False
    )
```

```python
import math

import jax
import jax.numpy as jnp
from jax import lax
from jax.sharding import PartitionSpec as P


def point_positions(point_ids, offsets, panel_len):
    first = jnp.where(point_ids[None, :] // panel_len == 0, offsets[:, 0:1], offsets[:, 1:2])
    return (first + point_ids[None, :] % panel_len).astype(jnp.float32)


def local(colloc, coefficients, occupied, offsets):
    row_count = lax.axis_size("row")
    col_count = lax.axis_size("col")
    col_index = lax.axis_index("col")
    spin_count, own_points, basis = colloc.shape
    slots = coefficients.shape[2]
    sub_rows = own_points // col_count
    points = own_points * row_count
    panel_len = points // 2
    screen_len = panel_len // 8
    col_width = basis // col_count
    row_width = basis // row_count
    norm_factor = 1.0 / math.sqrt(points)

    own_cols = lax.dynamic_slice_in_dim(colloc, col_index * col_width, col_width, 2)
    basis_cols = []
    for spin in range(spin_count):
        basis_cols.append(lax.all_gather(own_cols[spin], "row", axis=0, tiled=True))

    own_rows = lax.dynamic_slice_in_dim(colloc, col_index * sub_rows, sub_rows, 1)
    send = own_rows.reshape(spin_count, sub_rows, row_count, row_width).transpose(2, 0, 1, 3)
    regrouped = lax.all_to_all(send, "row", split_axis=0, concat_axis=0, tiled=True)
    basis_all = lax.all_gather(regrouped, "col", axis=0)

    partial_value = jnp.einsum(
        "xspm,smi->xspi", regrouped, coefficients, preferred_element_type=jnp.float32
    )
    received = lax.all_to_all(
        partial_value.astype(jnp.bfloat16), "row", split_axis=0, concat_axis=0, tiled=True
    )
    summed = jnp.sum(received.astype(jnp.float32), axis=0)
    occupied_mask = jnp.arange(slots, dtype=jnp.int32)[None, :] < occupied[:, None]
    orbitals_own = jnp.where(occupied_mask[:, None, :], summed, 0.0).astype(jnp.bfloat16)
    spread = jnp.broadcast_to(orbitals_own[None], (row_count,) + orbitals_own.shape)
    orbitals_group = lax.all_to_all(spread, "row", split_axis=0, concat_axis=0, tiled=True)
    orbitals_all = lax.all_gather(orbitals_group, "col", axis=0)

    def flat(x):
        return jnp.moveaxis(x, 2, 0).reshape(spin_count, points, x.shape[-1])

    orbitals_perm = flat(orbitals_all)
    basis_perm = flat(basis_all)
    ids = jnp.arange(points, dtype=jnp.int32)
    group_of, rest = ids // (row_count * sub_rows), ids % (row_count * sub_rows)
    perm_ids = rest // sub_rows * own_points + group_of * sub_rows + rest % sub_rows
    positions = point_positions(perm_ids, offsets, panel_len)
    kernel = 1.0 / (1.0 + jnp.abs(positions[:, :, None] - positions[:, None, :]) / screen_len)
    density = jnp.einsum(
        "spi,sqi->spq", orbitals_perm, orbitals_perm, preferred_element_type=jnp.float32
    )
    mixed_kernel = (kernel * density / slots).astype(jnp.bfloat16)
    weighted = jnp.einsum(
        "spq,sqn->spn", mixed_kernel, basis_perm, preferred_element_type=jnp.float32
    ).astype(jnp.bfloat16)
    weighted = (
        weighted.reshape(spin_count, col_count, row_count, sub_rows, -1)
        .transpose(0, 2, 1, 3, 4)
        .reshape(spin_count, points, -1)
    )
    blocks = [
        (
            jnp.einsum("pm,pn->mn", basis_cols[spin], weighted[spin], preferred_element_type=jnp.float32)
            * norm_factor
        ).astype(jnp.bfloat16)
        for spin in range(spin_count)
    ]
    return jnp.stack(blocks, axis=1)


def solution(mesh):
    placed = (P(None, "row", None), P(None, "row", None), P(), P())
    return jax.shard_map(
        local, mesh=mesh, in_specs=placed, out_specs=P("col", None, "row"), check_vma=False
    )
```

```python
import math

import jax
import jax.numpy as jnp
from jax import lax
from jax.sharding import PartitionSpec as P


def point_positions(point_ids, offsets, panel_len):
    first = jnp.where(point_ids[None, :] // panel_len == 0, offsets[:, 0:1], offsets[:, 1:2])
    return (first + point_ids[None, :] % panel_len).astype(jnp.float32)


def local(colloc, coefficients, occupied, offsets):
    row_count = lax.axis_size("row")
    col_count = lax.axis_size("col")
    col_index = lax.axis_index("col")
    spin_count, own_points, basis = colloc.shape
    slots = coefficients.shape[2]
    sub_rows = own_points // col_count
    points = own_points * row_count
    panel_len = points // 2
    screen_len = panel_len // 8
    col_width = basis // col_count
    row_width = basis // row_count
    norm_factor = 1.0 / math.sqrt(points)

    own_cols = lax.dynamic_slice_in_dim(colloc, col_index * col_width, col_width, 2)
    basis_cols = lax.all_gather(own_cols, "row", axis=1, tiled=True)

    send = colloc.reshape(spin_count, own_points, row_count, row_width).transpose(2, 0, 1, 3)
    basis_all = lax.all_to_all(send, "row", split_axis=0, concat_axis=0, tiled=True)
    basis_rows = jnp.moveaxis(basis_all, 1, 0).reshape(spin_count, points, row_width)
    regrouped = lax.dynamic_slice_in_dim(basis_all, col_index * sub_rows, sub_rows, 2)

    partial_value = jnp.einsum(
        "xspm,smi->xspi", regrouped, coefficients, preferred_element_type=jnp.float32
    )
    received = lax.all_to_all(
        partial_value.astype(jnp.bfloat16), "row", split_axis=0, concat_axis=0, tiled=True
    )
    summed = jnp.sum(received.astype(jnp.float32), axis=0)
    occupied_mask = jnp.arange(slots, dtype=jnp.int32)[None, :] < occupied[:, None]
    orbitals_own = jnp.where(occupied_mask[:, None, :], summed, 0.0).astype(jnp.bfloat16)
    spread = jnp.broadcast_to(orbitals_own[None], (row_count,) + orbitals_own.shape)
    orbitals_group = lax.all_to_all(spread, "row", split_axis=0, concat_axis=0, tiled=True)
    orbitals_all = lax.all_gather(orbitals_group, "col", axis=0)
    orbitals_nat = orbitals_all.transpose(2, 1, 0, 3, 4).reshape(spin_count, points, slots)

    positions = point_positions(jnp.arange(points, dtype=jnp.int32), offsets, panel_len)
    kernel = 1.0 / (1.0 + jnp.abs(positions[:, :, None] - positions[:, None, :]) / screen_len)
    density = jnp.einsum(
        "spi,sqi->spq", orbitals_nat, orbitals_nat, preferred_element_type=jnp.float32
    )
    mixed_kernel = (kernel * density / slots).astype(jnp.bfloat16)
    weighted = jnp.einsum(
        "spq,sqn->spn", mixed_kernel, basis_rows, preferred_element_type=jnp.float32
    ).astype(jnp.bfloat16)
    return (
        jnp.einsum("spm,spn->msn", basis_cols, weighted, preferred_element_type=jnp.float32)
        * norm_factor
    ).astype(jnp.bfloat16)


def solution(mesh):
    placed = (P(None, "row", None), P(None, "row", None), P(), P())
    return jax.shard_map(
        local, mesh=mesh, in_specs=placed, out_specs=P("col", None, "row"), check_vma=False
    )
```

```python
import math

import jax
import jax.numpy as jnp
from jax import lax
from jax.sharding import PartitionSpec as P


def point_positions(point_ids, offsets, panel_len):
    first = jnp.where(point_ids[None, :] // panel_len == 0, offsets[:, 0:1], offsets[:, 1:2])
    return (first + point_ids[None, :] % panel_len).astype(jnp.float32)


def gather_col(x, col_index, col_count):
    slot = jnp.arange(col_count, dtype=jnp.int32).reshape((col_count,) + (1,) * x.ndim)
    padded = jnp.where(slot == col_index, x[None], jnp.zeros_like(x)[None])
    return lax.psum(padded, "col")


def local(colloc, coefficients, occupied, offsets):
    row_count = lax.axis_size("row")
    col_count = lax.axis_size("col")
    col_index = lax.axis_index("col")
    spin_count, own_points, basis = colloc.shape
    slots = coefficients.shape[2]
    sub_rows = own_points // col_count
    points = own_points * row_count
    panel_len = points // 2
    screen_len = panel_len // 8
    col_width = basis // col_count
    row_width = basis // row_count
    norm_factor = 1.0 / math.sqrt(points)

    own_cols = lax.dynamic_slice_in_dim(colloc, col_index * col_width, col_width, 2)
    basis_cols = lax.all_gather(own_cols, "row", axis=1, tiled=True)

    own_rows = lax.dynamic_slice_in_dim(colloc, col_index * sub_rows, sub_rows, 1)
    send = own_rows.reshape(spin_count, sub_rows, row_count, row_width).transpose(2, 0, 1, 3)
    regrouped = lax.all_to_all(send, "row", split_axis=0, concat_axis=0, tiled=True)
    basis_all = gather_col(regrouped, col_index, col_count)
    basis_rows = basis_all.transpose(2, 1, 0, 3, 4).reshape(spin_count, points, row_width)

    partial_value = jnp.einsum(
        "xspm,smi->xspi", regrouped, coefficients, preferred_element_type=jnp.float32
    )
    received = lax.all_to_all(
        partial_value.astype(jnp.bfloat16), "row", split_axis=0, concat_axis=0, tiled=True
    )
    summed = jnp.sum(received.astype(jnp.float32), axis=0)
    occupied_mask = jnp.arange(slots, dtype=jnp.int32)[None, :] < occupied[:, None]
    orbitals_own = jnp.where(occupied_mask[:, None, :], summed, 0.0).astype(jnp.bfloat16)
    spread = jnp.broadcast_to(orbitals_own[None], (row_count,) + orbitals_own.shape)
    orbitals_group = lax.all_to_all(spread, "row", split_axis=0, concat_axis=0, tiled=True)
    orbitals_all = gather_col(orbitals_group, col_index, col_count)
    orbitals_nat = orbitals_all.transpose(2, 1, 0, 3, 4).reshape(spin_count, points, slots)

    positions = point_positions(jnp.arange(points, dtype=jnp.int32), offsets, panel_len)
    kernel = 1.0 / (1.0 + jnp.abs(positions[:, :, None] - positions[:, None, :]) / screen_len)
    density = jnp.einsum(
        "spi,sqi->spq", orbitals_nat, orbitals_nat, preferred_element_type=jnp.float32
    )
    mixed_kernel = (kernel * density / slots).astype(jnp.bfloat16)
    weighted = jnp.einsum(
        "spq,sqn->spn", mixed_kernel, basis_rows, preferred_element_type=jnp.float32
    ).astype(jnp.bfloat16)
    return (
        jnp.einsum("spm,spn->msn", basis_cols, weighted, preferred_element_type=jnp.float32)
        * norm_factor
    ).astype(jnp.bfloat16)


def solution(mesh):
    placed = (P(None, "row", None), P(None, "row", None), P(), P())
    return jax.shard_map(
        local, mesh=mesh, in_specs=placed, out_specs=P("col", None, "row"), check_vma=False
    )
```

```python
import math

import jax
import jax.numpy as jnp
from jax import lax
from jax.sharding import PartitionSpec as P


def point_positions(point_ids, offsets, panel_len):
    first = jnp.where(point_ids[None, :] // panel_len == 0, offsets[:, 0:1], offsets[:, 1:2])
    return (first + point_ids[None, :] % panel_len).astype(jnp.float32)


def local(colloc, coefficients, occupied, offsets):
    row_count = lax.axis_size("row")
    col_count = lax.axis_size("col")
    col_index = lax.axis_index("col")
    spin_count, own_points, basis = colloc.shape
    slots = coefficients.shape[2]
    sub_rows = own_points // col_count
    points = own_points * row_count
    panel_len = points // 2
    screen_len = panel_len // 8
    col_width = basis // col_count
    row_width = basis // row_count
    norm_factor = 1.0 / math.sqrt(points)

    own_cols = lax.dynamic_slice_in_dim(colloc, col_index * col_width, col_width, 2)
    basis_cols = lax.all_gather(own_cols, "row", axis=1, tiled=True)

    own_rows = lax.dynamic_slice_in_dim(colloc, col_index * sub_rows, sub_rows, 1)
    send = own_rows.reshape(spin_count, sub_rows, row_count, row_width).transpose(2, 0, 1, 3)
    regrouped = lax.all_to_all(send, "row", split_axis=0, concat_axis=0, tiled=True)

    partial_value = jnp.einsum(
        "xspm,smi->xspi", regrouped, coefficients, preferred_element_type=jnp.float32
    )
    received = lax.all_to_all(
        partial_value.astype(jnp.bfloat16), "row", split_axis=0, concat_axis=0, tiled=True
    )
    summed = jnp.sum(received.astype(jnp.float32), axis=0)
    occupied_mask = jnp.arange(slots, dtype=jnp.int32)[None, :] < occupied[:, None]
    orbitals_own = jnp.where(occupied_mask[:, None, :], summed, 0.0).astype(jnp.bfloat16)
    spread = jnp.broadcast_to(orbitals_own[None], (row_count,) + orbitals_own.shape)
    orbitals_group = lax.all_to_all(spread, "row", split_axis=0, concat_axis=0, tiled=True)
    orbitals_all = lax.all_gather(orbitals_group, "col", axis=0)
    orbitals_nat = orbitals_all.transpose(2, 1, 0, 3, 4).reshape(spin_count, points, slots)

    every = colloc.reshape(spin_count, own_points, row_count, row_width).transpose(2, 0, 1, 3)
    basis_all = lax.all_to_all(every, "row", split_axis=0, concat_axis=0, tiled=True)
    basis_rows = jnp.moveaxis(basis_all, 1, 0).reshape(spin_count, points, row_width)

    positions = point_positions(jnp.arange(points, dtype=jnp.int32), offsets, panel_len)
    kernel = 1.0 / (1.0 + jnp.abs(positions[:, :, None] - positions[:, None, :]) / screen_len)
    density = jnp.einsum(
        "spi,sqi->spq", orbitals_nat, orbitals_nat, preferred_element_type=jnp.float32
    )
    mixed_kernel = (kernel * density / slots).astype(jnp.bfloat16)
    weighted = jnp.einsum(
        "spq,sqn->spn", mixed_kernel, basis_rows, preferred_element_type=jnp.float32
    ).astype(jnp.bfloat16)
    return (
        jnp.einsum("spm,spn->msn", basis_cols, weighted, preferred_element_type=jnp.float32)
        * norm_factor
    ).astype(jnp.bfloat16)


def solution(mesh):
    placed = (P(None, "row", None), P(None, "row", None), P(), P())
    return jax.shard_map(
        local, mesh=mesh, in_specs=placed, out_specs=P("col", None, "row"), check_vma=False
    )
```

```python
import math

import jax
import jax.numpy as jnp
from jax import lax
from jax.sharding import PartitionSpec as P


def point_positions(point_ids, offsets, panel_len):
    first = jnp.where(point_ids[None, :] // panel_len == 0, offsets[:, 0:1], offsets[:, 1:2])
    return (first + point_ids[None, :] % panel_len).astype(jnp.float32)


def local(colloc, coefficients, occupied, offsets):
    row_count = lax.axis_size(ROW)
    col_count = lax.axis_size("col")
    col_index = lax.axis_index("col")
    spin_count, own_points, basis = colloc.shape
    slots = coefficients.shape[2]
    sub_rows = own_points // col_count
    points = own_points * row_count
    panel_len = points // 2
    screen_len = panel_len // 8
    col_width = basis // col_count
    row_width = basis // row_count
    norm_factor = 1.0 / math.sqrt(points)

    own_cols = lax.dynamic_slice_in_dim(colloc, col_index * col_width, col_width, 2)
    chip_cols = lax.all_gather(own_cols, "rz", axis=1, tiled=True)
    basis_cols = lax.all_gather(chip_cols, "core", axis=0)
    core_count = basis_cols.shape[0]
    basis_cols = basis_cols.reshape(core_count, spin_count, row_count // core_count, own_points, col_width)

    own_rows = lax.dynamic_slice_in_dim(colloc, col_index * sub_rows, sub_rows, 1)
    send = own_rows.reshape(spin_count, sub_rows, row_count, row_width).transpose(2, 0, 1, 3)
    regrouped = lax.all_to_all(send, ROW, split_axis=0, concat_axis=0, tiled=True)

    partial_value = jnp.einsum(
        "xspm,smi->xspi", regrouped, coefficients, preferred_element_type=jnp.float32
    )
    received = lax.all_to_all(
        partial_value.astype(jnp.bfloat16), ROW, split_axis=0, concat_axis=0, tiled=True
    )
    summed = jnp.sum(received.astype(jnp.float32), axis=0)
    occupied_mask = jnp.arange(slots, dtype=jnp.int32)[None, :] < occupied[:, None]
    orbitals_own = jnp.where(occupied_mask[:, None, :], summed, 0.0).astype(jnp.bfloat16)
    spread = jnp.broadcast_to(orbitals_own[None], (row_count,) + orbitals_own.shape)
    orbitals_group = lax.all_to_all(spread, ROW, split_axis=0, concat_axis=0, tiled=True)
    orbitals_all = lax.all_gather(orbitals_group, "col", axis=0)
    orbitals_nat = orbitals_all.transpose(2, 1, 0, 3, 4).reshape(spin_count, points, slots)

    every = colloc.reshape(spin_count, own_points, row_count, row_width).transpose(2, 0, 1, 3)
    basis_all = lax.all_to_all(every, ROW, split_axis=0, concat_axis=0, tiled=True)
    basis_rows = jnp.moveaxis(basis_all, 1, 0).reshape(spin_count, points, row_width)

    positions = point_positions(jnp.arange(points, dtype=jnp.int32), offsets, panel_len)
    kernel = 1.0 / (1.0 + jnp.abs(positions[:, :, None] - positions[:, None, :]) / screen_len)
    density = jnp.einsum(
        "spi,sqi->spq", orbitals_nat, orbitals_nat, preferred_element_type=jnp.float32
    )
    mixed_kernel = (kernel * density / slots).astype(jnp.bfloat16)
    weighted = jnp.einsum(
        "spq,sqn->spn", mixed_kernel, basis_rows, preferred_element_type=jnp.float32
    ).astype(jnp.bfloat16)
    weighted = weighted.reshape(spin_count, row_count // core_count, core_count, own_points, -1)
    return (
        jnp.einsum("bsrjm,srbjn->msn", basis_cols, weighted, preferred_element_type=jnp.float32)
        * norm_factor
    ).astype(jnp.bfloat16)


ROW = ("rz", "core")


def solution(mesh):
    rows, cols = mesh.devices.shape
    fine = jax.sharding.Mesh(mesh.devices.reshape(rows // 2, 2, cols), ("rz", "core", "col"))
    placed = (P(None, ROW, None), P(None, ROW, None), P(), P())
    return jax.shard_map(
        local, mesh=fine, in_specs=placed, out_specs=P("col", None, ROW), check_vma=False
    )
```

```python
import math

import jax
import jax.numpy as jnp
from jax import lax
from jax.sharding import PartitionSpec as P


def point_positions(point_ids, offsets, panel_len):
    first = jnp.where(point_ids[None, :] // panel_len == 0, offsets[:, 0:1], offsets[:, 1:2])
    return (first + point_ids[None, :] % panel_len).astype(jnp.float32)


def gather_col(x, col_count):
    spread = jnp.broadcast_to(x[None], (col_count,) + x.shape)
    return lax.all_to_all(spread, "col", split_axis=0, concat_axis=0, tiled=True)


def local(colloc, coefficients, occupied, offsets):
    row_count = lax.axis_size("row")
    col_count = lax.axis_size("col")
    col_index = lax.axis_index("col")
    spin_count, own_points, basis = colloc.shape
    slots = coefficients.shape[2]
    sub_rows = own_points // col_count
    points = own_points * row_count
    panel_len = points // 2
    screen_len = panel_len // 8
    col_width = basis // col_count
    row_width = basis // row_count
    norm_factor = 1.0 / math.sqrt(points)

    own_cols = lax.dynamic_slice_in_dim(colloc, col_index * col_width, col_width, 2)
    basis_cols = lax.all_gather(own_cols, "row", axis=1, tiled=True)

    own_rows = lax.dynamic_slice_in_dim(colloc, col_index * sub_rows, sub_rows, 1)
    send = own_rows.reshape(spin_count, sub_rows, row_count, row_width).transpose(2, 0, 1, 3)
    regrouped = lax.all_to_all(send, "row", split_axis=0, concat_axis=0, tiled=True)

    partial_value = jnp.einsum(
        "xspm,smi->xspi", regrouped, coefficients, preferred_element_type=jnp.float32
    )
    received = lax.all_to_all(
        partial_value.astype(jnp.bfloat16), "row", split_axis=0, concat_axis=0, tiled=True
    )
    summed = jnp.sum(received.astype(jnp.float32), axis=0)
    occupied_mask = jnp.arange(slots, dtype=jnp.int32)[None, :] < occupied[:, None]
    orbitals_own = jnp.where(occupied_mask[:, None, :], summed, 0.0).astype(jnp.bfloat16)
    spread = jnp.broadcast_to(orbitals_own[None], (row_count,) + orbitals_own.shape)
    orbitals_group = lax.all_to_all(spread, "row", split_axis=0, concat_axis=0, tiled=True)
    both = gather_col(jnp.concatenate([orbitals_group, regrouped], axis=3), col_count)
    orbitals_all = both[..., :slots]
    basis_rows = both[..., slots:].transpose(2, 1, 0, 3, 4).reshape(spin_count, points, row_width)
    orbitals_nat = orbitals_all.transpose(2, 1, 0, 3, 4).reshape(spin_count, points, slots)

    positions = point_positions(jnp.arange(points, dtype=jnp.int32), offsets, panel_len)
    kernel = 1.0 / (1.0 + jnp.abs(positions[:, :, None] - positions[:, None, :]) / screen_len)
    density = jnp.einsum(
        "spi,sqi->spq", orbitals_nat, orbitals_nat, preferred_element_type=jnp.float32
    )
    mixed_kernel = (kernel * density / slots).astype(jnp.bfloat16)
    weighted = jnp.einsum(
        "spq,sqn->spn", mixed_kernel, basis_rows, preferred_element_type=jnp.float32
    ).astype(jnp.bfloat16)
    return (
        jnp.einsum("spm,spn->msn", basis_cols, weighted, preferred_element_type=jnp.float32)
        * norm_factor
    ).astype(jnp.bfloat16)


def solution(mesh):
    placed = (P(None, "row", None), P(None, "row", None), P(), P())
    return jax.shard_map(
        local, mesh=mesh, in_specs=placed, out_specs=P("col", None, "row"), check_vma=False
    )
```

```python
import math

import jax
import jax.numpy as jnp
from jax import lax
from jax.sharding import PartitionSpec as P


def point_positions(point_ids, offsets, panel_len):
    first = jnp.where(point_ids[None, :] // panel_len == 0, offsets[:, 0:1], offsets[:, 1:2])
    return (first + point_ids[None, :] % panel_len).astype(jnp.float32)


def gather_col(x, col_count):
    spread = jnp.broadcast_to(x[None], (col_count,) + x.shape)
    return lax.all_to_all(spread, "col", split_axis=0, concat_axis=0, tiled=True)


def local(colloc, coefficients, occupied, offsets):
    row_count = lax.axis_size("row")
    col_count = lax.axis_size("col")
    col_index = lax.axis_index("col")
    spin_count, own_points, basis = colloc.shape
    slots = coefficients.shape[2]
    sub_rows = own_points // col_count
    points = own_points * row_count
    panel_len = points // 2
    screen_len = panel_len // 8
    col_width = basis // col_count
    row_width = basis // row_count
    norm_factor = 1.0 / math.sqrt(points)

    own_cols = lax.dynamic_slice_in_dim(colloc, col_index * col_width, col_width, 2)
    basis_cols = lax.all_gather(own_cols, "row", axis=1, tiled=True)

    own_rows = lax.dynamic_slice_in_dim(colloc, col_index * sub_rows, sub_rows, 1)
    send = own_rows.reshape(spin_count, sub_rows, row_count, row_width).transpose(2, 0, 1, 3)
    regrouped = lax.all_to_all(send, "row", split_axis=0, concat_axis=0, tiled=True)
    basis_all = lax.all_gather(regrouped, "col", axis=0)
    basis_rows = basis_all.transpose(2, 1, 0, 3, 4).reshape(spin_count, points, row_width)

    partial_value = jnp.einsum(
        "xspm,smi->xspi", regrouped, coefficients, preferred_element_type=jnp.float32
    )
    received = lax.all_to_all(
        partial_value.astype(jnp.bfloat16), "row", split_axis=0, concat_axis=0, tiled=True
    )
    summed = jnp.sum(received.astype(jnp.float32), axis=0)
    occupied_mask = jnp.arange(slots, dtype=jnp.int32)[None, :] < occupied[:, None]
    orbitals_own = jnp.where(occupied_mask[:, None, :], summed, 0.0).astype(jnp.bfloat16)
    spread = jnp.broadcast_to(orbitals_own[None], (row_count,) + orbitals_own.shape)
    orbitals_group = lax.all_to_all(spread, "row", split_axis=0, concat_axis=0, tiled=True)
    orbitals_all = gather_col(orbitals_group, col_count)
    orbitals_nat = orbitals_all.transpose(2, 1, 0, 3, 4).reshape(spin_count, points, slots)

    positions = point_positions(jnp.arange(points, dtype=jnp.int32), offsets, panel_len)
    kernel = 1.0 / (1.0 + jnp.abs(positions[:, :, None] - positions[:, None, :]) / screen_len)
    density = jnp.einsum(
        "spi,sqi->spq", orbitals_nat, orbitals_nat, preferred_element_type=jnp.float32
    )
    mixed_kernel = (kernel * density / slots).astype(jnp.bfloat16)
    weighted = jnp.einsum(
        "spq,sqn->spn", mixed_kernel, basis_rows, preferred_element_type=jnp.float32
    ).astype(jnp.bfloat16)
    return (
        jnp.einsum("spm,spn->msn", basis_cols, weighted, preferred_element_type=jnp.float32)
        * norm_factor
    ).astype(jnp.bfloat16)


def solution(mesh):
    placed = (P(None, "row", None), P(None, "row", None), P(), P())
    return jax.shard_map(
        local, mesh=mesh, in_specs=placed, out_specs=P("col", None, "row"), check_vma=False
    )
```

```python
import math

import jax
import jax.numpy as jnp
from jax import lax
from jax.sharding import PartitionSpec as P


def point_positions(point_ids, offsets, panel_len):
    first = jnp.where(point_ids[None, :] // panel_len == 0, offsets[:, 0:1], offsets[:, 1:2])
    return (first + point_ids[None, :] % panel_len).astype(jnp.float32)


def gather_col(x, col_count):
    spread = jnp.broadcast_to(x[None], (col_count,) + x.shape)
    return lax.all_to_all(spread, "col", split_axis=0, concat_axis=0, tiled=True)


def local(colloc, coefficients, occupied, offsets):
    row_count = lax.axis_size("row")
    col_count = lax.axis_size("col")
    col_index = lax.axis_index("col")
    spin_count, own_points, basis = colloc.shape
    slots = coefficients.shape[2]
    sub_rows = own_points // col_count
    points = own_points * row_count
    panel_len = points // 2
    screen_len = panel_len // 8
    col_width = basis // col_count
    row_width = basis // row_count
    norm_factor = 1.0 / math.sqrt(points)

    own_cols = lax.dynamic_slice_in_dim(colloc, col_index * col_width, col_width, 2)
    basis_cols = lax.all_gather(own_cols, "row", axis=1, tiled=True)

    own_rows = lax.dynamic_slice_in_dim(colloc, col_index * sub_rows, sub_rows, 1)
    send = own_rows.reshape(spin_count, sub_rows, row_count, row_width).transpose(2, 0, 1, 3)
    regrouped = lax.all_to_all(send, "row", split_axis=0, concat_axis=0, tiled=True)
    basis_all = gather_col(regrouped, col_count)
    basis_rows = basis_all.transpose(2, 1, 0, 3, 4).reshape(spin_count, points, row_width)

    partial_value = jnp.einsum(
        "xspm,smi->xspi", regrouped, coefficients, preferred_element_type=jnp.float32
    )
    received = lax.all_to_all(
        partial_value.astype(jnp.bfloat16), "row", split_axis=0, concat_axis=0, tiled=True
    )
    summed = jnp.sum(received.astype(jnp.float32), axis=0)
    occupied_mask = jnp.arange(slots, dtype=jnp.int32)[None, :] < occupied[:, None]
    orbitals_own = jnp.where(occupied_mask[:, None, :], summed, 0.0).astype(jnp.bfloat16)
    spread = jnp.broadcast_to(orbitals_own[None], (row_count,) + orbitals_own.shape)
    orbitals_group = lax.all_to_all(spread, "row", split_axis=0, concat_axis=0, tiled=True)
    orbitals_first = gather_col(orbitals_group[:, :1], col_count)
    orbitals_rest = lax.all_gather(orbitals_group[:, 1:], "col", axis=0)
    orbitals_all = jnp.concatenate([orbitals_first, orbitals_rest], axis=2)
    orbitals_nat = orbitals_all.transpose(2, 1, 0, 3, 4).reshape(spin_count, points, slots)

    positions = point_positions(jnp.arange(points, dtype=jnp.int32), offsets, panel_len)
    kernel = 1.0 / (1.0 + jnp.abs(positions[:, :, None] - positions[:, None, :]) / screen_len)
    density = jnp.einsum(
        "spi,sqi->spq", orbitals_nat, orbitals_nat, preferred_element_type=jnp.float32
    )
    mixed_kernel = (kernel * density / slots).astype(jnp.bfloat16)
    weighted = jnp.einsum(
        "spq,sqn->spn", mixed_kernel, basis_rows, preferred_element_type=jnp.float32
    ).astype(jnp.bfloat16)
    return (
        jnp.einsum("spm,spn->msn", basis_cols, weighted, preferred_element_type=jnp.float32)
        * norm_factor
    ).astype(jnp.bfloat16)


def solution(mesh):
    placed = (P(None, "row", None), P(None, "row", None), P(), P())
    return jax.shard_map(
        local, mesh=mesh, in_specs=placed, out_specs=P("col", None, "row"), check_vma=False
    )
```

```python
import math

import jax
import jax.numpy as jnp
from jax import lax
from jax.sharding import PartitionSpec as P


def point_positions(point_ids, offsets, panel_len):
    first = jnp.where(point_ids[None, :] // panel_len == 0, offsets[:, 0:1], offsets[:, 1:2])
    return (first + point_ids[None, :] % panel_len).astype(jnp.float32)


def gather_col(x, col_count):
    spread = jnp.broadcast_to(x[None], (col_count,) + x.shape)
    return lax.all_to_all(spread, "col", split_axis=0, concat_axis=0, tiled=True)


def local(colloc, coefficients, occupied, offsets):
    row_count = lax.axis_size("row")
    col_count = lax.axis_size("col")
    col_index = lax.axis_index("col")
    spin_count, own_points, basis = colloc.shape
    slots = coefficients.shape[2]
    sub_rows = own_points // col_count
    points = own_points * row_count
    panel_len = points // 2
    screen_len = panel_len // 8
    col_width = basis // col_count
    row_width = basis // row_count
    norm_factor = 1.0 / math.sqrt(points)

    own_cols = lax.dynamic_slice_in_dim(colloc, col_index * col_width, col_width, 2)
    basis_cols = lax.all_gather(own_cols, "row", axis=1, tiled=True)

    own_rows = lax.dynamic_slice_in_dim(colloc, col_index * sub_rows, sub_rows, 1)
    send = own_rows.reshape(spin_count, sub_rows, row_count, row_width).transpose(2, 0, 1, 3)
    regrouped = lax.all_to_all(send, "row", split_axis=0, concat_axis=0, tiled=True)
    basis_all = gather_col(regrouped, col_count)
    basis_rows = basis_all.transpose(2, 1, 0, 3, 4).reshape(spin_count, points, row_width)

    partial_value = jnp.einsum(
        "xspm,smi->xspi", regrouped, coefficients, preferred_element_type=jnp.float32
    )
    received = lax.all_to_all(
        partial_value.astype(jnp.bfloat16), "row", split_axis=0, concat_axis=0, tiled=True
    )
    summed = jnp.sum(received.astype(jnp.float32), axis=0)
    occupied_mask = jnp.arange(slots, dtype=jnp.int32)[None, :] < occupied[:, None]
    orbitals_own = jnp.where(occupied_mask[:, None, :], summed, 0.0).astype(jnp.bfloat16)
    spread = jnp.broadcast_to(orbitals_own[None], (row_count,) + orbitals_own.shape)
    orbitals_group = lax.all_to_all(spread, "row", split_axis=0, concat_axis=0, tiled=True)
    orbitals_first = gather_col(orbitals_group[:, :1], col_count)
    orbitals_rest = lax.all_gather(orbitals_group[:, 1:], "col", axis=0)

    positions = point_positions(jnp.arange(points, dtype=jnp.int32), offsets, panel_len)
    kernel = 1.0 / (1.0 + jnp.abs(positions[:, :, None] - positions[:, None, :]) / screen_len)
    blocks = []
    for spin, orbitals_all in enumerate((orbitals_first, orbitals_rest)):
        orbitals_nat = orbitals_all[:, :, 0].transpose(1, 0, 2, 3).reshape(points, slots)
        density = jnp.einsum(
            "pi,qi->pq", orbitals_nat, orbitals_nat, preferred_element_type=jnp.float32
        )
        mixed_kernel = (kernel[spin] * density / slots).astype(jnp.bfloat16)
        weighted = jnp.einsum(
            "pq,qn->pn", mixed_kernel, basis_rows[spin], preferred_element_type=jnp.float32
        ).astype(jnp.bfloat16)
        blocks.append(
            (
                jnp.einsum("pm,pn->mn", basis_cols[spin], weighted, preferred_element_type=jnp.float32)
                * norm_factor
            ).astype(jnp.bfloat16)
        )
    return jnp.stack(blocks, axis=1)


def solution(mesh):
    placed = (P(None, "row", None), P(None, "row", None), P(), P())
    return jax.shard_map(
        local, mesh=mesh, in_specs=placed, out_specs=P("col", None, "row"), check_vma=False
    )
```
